128 devices in a mesh: freq: 8 (over z_hi, x), blk: 16 (over y, z_lo, core).
Axes of the slice: x: 4, y: 4, z: 4 (z_hi: 2, z_lo: 2; z = z_hi * 2 + z_lo), core: 2. Of those that a mesh axis runs over, the one named last changes fastest.
Arguments:
- traces: bfloat16 [2048, 2048, 256], P('blk', 'freq'), may hold values from -6 to 6
- signature: float32 [8, 2], P('freq'), may hold values from 0.5 to 1.5
Outputs:
- multiples: float32 [8, 2, 2048, 2048], P('freq', None, 'blk')
The draws below stay inside these ranges and needn't reach their ends.
All inputs are finite; a program needn't handle non-finite values.
Results may differ from the reference program's by a relative error of at most 0.0035.
Values sent between devices are 32-bit elements; how exact they have to be, the bound alone decides.
No kernel may reach another device: no remote copies, remote signals or barrier semaphores. Data moves between devices by JAX's collectives and lax.ppermute only.
A program may use at most 256 MiB of HBM per device.

```python
import math
import jax
import jax.numpy as jnp
from jax import lax

N = 2048
NT = 256
BIN0 = 4
BINSTEP = 3
F = 8
N_BLK = 16


def block_levels(stream_key, shape, split, low, high):
    gain = 1.0
    for position, parts in split:
        steps = jax.random.uniform(jax.random.fold_in(jax.random.fold_in(stream_key, 6), position), (parts,), jnp.float32, low / len(split), high / len(split))
        gain = gain * jnp.repeat(jnp.exp(steps), shape[position] // parts).reshape((-1,) + (1,) * (len(shape) - 1 - position))
    return gain


def centred(own_key, dims, scale, bound, pieces=(), kind=jnp.bfloat16):
    values = scale * jax.random.normal(own_key, dims, jnp.float32)
    if pieces:
        values = values * block_levels(own_key, dims, pieces, -0.22, 0.18)
    return jnp.clip(values, -bound, bound).astype(kind)


def setup_inputs(seed: int = 0) -> dict:
    arg_keys = jax.random.split(jax.random.key(seed), 3)
    traces = centred(arg_keys[0], (N, N, NT), 1.0, 6.0, ((0, 16), (1, 8)))
    signature = jnp.clip(0.5 + 1.0 * jax.random.uniform(arg_keys[1], (F, 2), jnp.float32) ** block_levels(arg_keys[1], (F, 2), ((0, 8),), -0.2, 0.2), 0.5, 1.5)
    return dict(traces=traces, signature=signature)


def make_table(freqs, samples):
    bins = BIN0 + BINSTEP * jnp.arange(freqs, dtype=jnp.int32)
    steps = jnp.arange(samples, dtype=jnp.int32)
    phase = steps[:, None] * bins[None, :] % samples
    angle = phase.astype(jnp.float32) * (2.0 * math.pi / samples)
    scale = 1.0 / math.sqrt(samples)
    table = jnp.concatenate([jnp.cos(angle) * scale, -jnp.sin(angle) * scale], axis=1)
    return table.astype(jnp.bfloat16)

def reference(traces, signature):
    table = make_table(F, NT)
    rows_blk = N // N_BLK
    blocks = traces.reshape(N_BLK, rows_blk, N, NT)

    def project(block):
        flat = jnp.dot(block.reshape(rows_blk * N, NT), table, preferred_element_type=jnp.float32)
        return flat.reshape(rows_blk, N, 2 * F)
    spectra = lax.map(project, blocks).reshape(N, N, 2 * F)
    hp = lax.Precision.HIGHEST
    scale = 1.0 / math.sqrt(N)
    results = []
    for j in range(F):
        d_re = spectra[:, :, j]
        d_im = spectra[:, :, F + j]
        p_re = jnp.dot(d_re, d_re, precision=hp) - jnp.dot(d_im, d_im, precision=hp)
        p_im = jnp.dot(d_re, d_im, precision=hp) + jnp.dot(d_im, d_re, precision=hp)
        w_re = signature[j, 0]
        w_im = signature[j, 1]
        m_re = -(w_re * p_re - w_im * p_im) * scale
        m_im = -(w_re * p_im + w_im * p_re) * scale
        results.append(jnp.stack([m_re, m_im], axis=0))
    return jnp.stack(results, axis=0)
```

```python
import math

import jax
import jax.numpy as jnp
from jax import lax
from jax.sharding import PartitionSpec as P

BIN0 = 4
BINSTEP = 3
GROUP = 4


def make_table(freqs, samples):
    bins = BIN0 + BINSTEP * jnp.arange(freqs, dtype=jnp.int32)
    steps = jnp.arange(samples, dtype=jnp.int32)
    phase = steps[:, None] * bins[None, :] % samples
    angle = phase.astype(jnp.float32) * (2.0 * math.pi / samples)
    scale = 1.0 / math.sqrt(samples)
    table = jnp.concatenate([jnp.cos(angle) * scale, -jnp.sin(angle) * scale], axis=1)
    return table.astype(jnp.bfloat16)


def xor_perm(n, m):
    return [(i, i ^ m) for i in range(n)]


def shift_perm(n, s):
    return [(i, (i + s) % n) for i in range(n)]


def on_device(traces, signature):
    src_rows, rec_cols, samples = traces.shape
    freqs = lax.axis_size("freq")
    nblk = lax.axis_size("blk")
    ny = nblk // GROUP
    assert ny == 4 and nblk % GROUP == 0
    table = make_table(freqs, samples)
    projected = jnp.einsum("srt,tc->csr", traces, table, preferred_element_type=jnp.float32)
    projected = projected.reshape(2, freqs, src_rows, rec_cols)
    spectra = lax.all_to_all(projected, "freq", split_axis=1, concat_axis=3, tiled=True)
    own = spectra[:, 0]
    n = own.shape[2]
    rb = src_rows
    gw = GROUP * rb
    cw = n // GROUP

    b = lax.axis_index("blk")
    p = b % GROUP
    y = b // GROUP

    q1 = lax.ppermute(own, "blk", xor_perm(nblk, 1))
    q2 = lax.ppermute(own, "blk", xor_perm(nblk, 2))
    q3 = lax.ppermute(q2, "blk", xor_perm(nblk, 1))
    rows = jnp.concatenate([own, q1, q2, q3], axis=1)

    piece = lax.dynamic_slice_in_dim(rows, p * cw, cw, axis=2)

    l5 = rows.reshape(2, gw, ny, GROUP, rb)
    lx = jnp.concatenate(
        [lax.dynamic_slice_in_dim(l5, p ^ m, 1, axis=3) for m in range(GROUP)], axis=3
    ).reshape(2, gw, n)

    def contrib(g, pc, lo, hi):
        lg = lax.dynamic_slice_in_dim(lx, g * gw + lo * rb, (hi - lo) * rb, axis=2)
        return jnp.einsum(
            "aik,bkj->abij", lg, pc,
            precision=lax.Precision.HIGH, preferred_element_type=jnp.float32,
        )

    up = shift_perm(nblk, GROUP)
    dn = shift_perm(nblk, -GROUP)
    r_up = lax.ppermute(piece, "blk", up)
    r_dn = lax.ppermute(piece, "blk", dn)
    half = gw // 2
    f_up = lax.ppermute(r_up[:, :half], "blk", up)
    f_dn = lax.ppermute(r_dn[:, half:], "blk", dn)

    t = contrib(y, piece, 0, GROUP)
    t = t + contrib((y - 1) % ny, r_up, 0, GROUP)
    t = t + contrib((y + 1) % ny, r_dn, 0, GROUP)
    t = t + contrib((y + 2) % ny, f_up, 0, GROUP // 2)
    t = t + contrib((y + 2) % ny, f_dn, GROUP // 2, GROUP)

    prod_re = t[0, 0] - t[1, 1]
    prod_im = t[0, 1] + t[1, 0]
    scale = 1.0 / math.sqrt(n)
    w_re = signature[0, 0]
    w_im = signature[0, 1]
    out_re = -(w_re * prod_re - w_im * prod_im) * scale
    out_im = -(w_re * prod_im + w_im * prod_re) * scale
    blk_out = jnp.stack([out_re, out_im], axis=0)

    parts = [blk_out[:, :rb]]
    for m in range(1, GROUP):
        parts.append(lax.ppermute(blk_out[:, m * rb:(m + 1) * rb], "blk", xor_perm(nblk, m)))
    stacked = jnp.stack(parts, axis=0)
    ordered = [lax.dynamic_index_in_dim(stacked, p ^ i, 0, keepdims=False) for i in range(GROUP)]
    out = jnp.concatenate(ordered, axis=2)
    return out[None]


def solution(mesh):
    return jax.shard_map(
        on_device,
        mesh=mesh,
        in_specs=(P("blk", "freq", None), P("freq", None)),
        out_specs=P("freq", None, "blk", None),
        check_vma=False,
    )
```

```python
import math

import jax
import jax.numpy as jnp
from jax import lax
from jax.sharding import PartitionSpec as P

BIN0 = 4
BINSTEP = 3
GROUP = 4


def make_table(freqs, samples):
    bins = BIN0 + BINSTEP * jnp.arange(freqs, dtype=jnp.int32)
    steps = jnp.arange(samples, dtype=jnp.int32)
    phase = steps[:, None] * bins[None, :] % samples
    angle = phase.astype(jnp.float32) * (2.0 * math.pi / samples)
    scale = 1.0 / math.sqrt(samples)
    table = jnp.concatenate([jnp.cos(angle) * scale, -jnp.sin(angle) * scale], axis=1)
    return table.astype(jnp.bfloat16)


def xor_perm(n, m):
    return [(i, i ^ m) for i in range(n)]


def shift_perm(n, s):
    return [(i, (i + s) % n) for i in range(n)]


def on_device(traces, signature):
    src_rows, rec_cols, samples = traces.shape
    freqs = lax.axis_size("freq")
    nblk = lax.axis_size("blk")
    ny = nblk // GROUP
    assert ny == 4 and nblk % GROUP == 0
    table = make_table(freqs, samples)
    projected = jnp.einsum("srt,tc->csr", traces, table, preferred_element_type=jnp.float32)
    projected = projected.reshape(2, freqs, src_rows, rec_cols)
    spectra = lax.all_to_all(projected, "freq", split_axis=1, concat_axis=3, tiled=True)
    own = spectra[:, 0]
    n = own.shape[2]
    rb = src_rows
    gw = GROUP * rb
    cw = n // GROUP

    b = lax.axis_index("blk")
    p = b % GROUP
    y = b // GROUP

    def cols(x, i):
        return lax.dynamic_slice_in_dim(x, i * cw, cw, axis=2)

    q1 = lax.ppermute(own, "blk", xor_perm(nblk, 1))
    c2 = lax.ppermute(cols(own, p ^ 2), "blk", xor_perm(nblk, 2))
    c3 = lax.ppermute(cols(own, p ^ 3), "blk", xor_perm(nblk, 3))
    rest = jnp.concatenate([cols(own, p ^ 2 ^ m) for m in range(1, GROUP)], axis=2)
    rest = lax.ppermute(rest, "blk", xor_perm(nblk, 2))
    q2 = jnp.zeros_like(own)
    q2 = lax.dynamic_update_slice_in_dim(q2, c2, p * cw, axis=2)
    for m in range(1, GROUP):
        q2 = lax.dynamic_update_slice_in_dim(q2, rest[:, :, (m - 1) * cw:m * cw], (p ^ m) * cw, axis=2)
    q3 = lax.ppermute(q2, "blk", xor_perm(nblk, 1))
    rows = jnp.concatenate([own, q1, q2, q3], axis=1)

    l5 = rows.reshape(2, gw, ny, GROUP, rb)
    lx = jnp.concatenate(
        [lax.dynamic_slice_in_dim(l5, p ^ m, 1, axis=3) for m in range(GROUP)], axis=3
    ).reshape(2, gw, n)

    def contrib(g, pc, lo, hi):
        lg = lax.dynamic_slice_in_dim(lx, g * gw + lo * rb, (hi - lo) * rb, axis=2)
        return jnp.einsum(
            "aik,bkj->abij", lg, pc,
            precision=lax.Precision.HIGH, preferred_element_type=jnp.float32,
        )

    part_a = jnp.concatenate([cols(own, p), cols(q1, p)], axis=1)
    part_b = jnp.concatenate([c2, c3], axis=1)
    up = shift_perm(nblk, GROUP)
    dn = shift_perm(nblk, -GROUP)
    ua = lax.ppermute(part_a, "blk", up)
    da = lax.ppermute(part_a, "blk", dn)
    ub = lax.ppermute(part_b, "blk", up)
    db = lax.ppermute(part_b, "blk", dn)
    fa = lax.ppermute(ua, "blk", up)
    fb = lax.ppermute(db, "blk", dn)

    half = GROUP // 2
    t = contrib(y, part_a, 0, half) + contrib(y, part_b, half, GROUP)
    t = t + contrib((y - 1) % ny, ua, 0, half) + contrib((y + 1) % ny, da, 0, half)
    t = t + contrib((y - 1) % ny, ub, half, GROUP) + contrib((y + 1) % ny, db, half, GROUP)
    t = t + contrib((y + 2) % ny, fa, 0, half) + contrib((y + 2) % ny, fb, half, GROUP)

    prod_re = t[0, 0] - t[1, 1]
    prod_im = t[0, 1] + t[1, 0]
    scale = 1.0 / math.sqrt(n)
    w_re = signature[0, 0]
    w_im = signature[0, 1]
    out_re = -(w_re * prod_re - w_im * prod_im) * scale
    out_im = -(w_re * prod_im + w_im * prod_re) * scale
    blk_out = jnp.stack([out_re, out_im], axis=0)

    parts = [blk_out[:, :rb]]
    for m in range(1, GROUP):
        parts.append(lax.ppermute(blk_out[:, m * rb:(m + 1) * rb], "blk", xor_perm(nblk, m)))
    stacked = jnp.stack(parts, axis=0)
    ordered = [lax.dynamic_index_in_dim(stacked, p ^ i, 0, keepdims=False) for i in range(GROUP)]
    out = jnp.concatenate(ordered, axis=2)
    return out[None]


def solution(mesh):
    return jax.shard_map(
        on_device,
        mesh=mesh,
        in_specs=(P("blk", "freq", None), P("freq", None)),
        out_specs=P("freq", None, "blk", None),
        check_vma=False,
    )
```

```python
import math

import jax
import jax.numpy as jnp
from jax import lax
from jax.sharding import PartitionSpec as P


BIN0 = 4
BINSTEP = 3
GROUP = 4


def make_table(freqs, samples):
    bins = BIN0 + BINSTEP * jnp.arange(freqs, dtype=jnp.int32)
    steps = jnp.arange(samples, dtype=jnp.int32)
    phase = steps[:, None] * bins[None, :] % samples
    angle = phase.astype(jnp.float32) * (2.0 * math.pi / samples)
    scale = 1.0 / math.sqrt(samples)
    table = jnp.concatenate([jnp.cos(angle) * scale, -jnp.sin(angle) * scale], axis=1)
    return table.astype(jnp.bfloat16)


def xor_perm(n, m):
    return [(i, i ^ m) for i in range(n)]


def shift_perm(n, s):
    return [(i, (i + s) % n) for i in range(n)]


def send(x, perm):
    return lax.ppermute(x, "blk", perm)


def on_device(traces, signature):
    src_rows, rec_cols, samples = traces.shape
    freqs = lax.axis_size("freq")
    nblk = lax.axis_size("blk")
    ny = nblk // GROUP
    assert ny == 4 and nblk % GROUP == 0
    table = make_table(freqs, samples)
    projected = jnp.einsum("srt,tc->csr", traces, table, preferred_element_type=jnp.float32)
    projected = projected.reshape(2, freqs, src_rows, rec_cols)
    spectra = lax.all_to_all(projected, "freq", split_axis=1, concat_axis=3, tiled=True)
    own = spectra[:, 0]
    n = own.shape[2]
    rb = src_rows
    gw = GROUP * rb
    cw = n // GROUP

    b = lax.axis_index("blk")
    p = b % GROUP
    y = b // GROUP

    def cols(x, i):
        return lax.dynamic_slice_in_dim(x, i * cw, cw, axis=2)

    q1 = send(own, xor_perm(nblk, 1))
    c2 = send(cols(own, p ^ 2), xor_perm(nblk, 2))
    c3 = send(cols(own, p ^ 3), xor_perm(nblk, 3))
    rest = jnp.concatenate([cols(own, p ^ 2 ^ m) for m in range(1, GROUP)], axis=2)
    rest, _, _ = lax.optimization_barrier((rest, c2, c3))
    rest = send(rest, xor_perm(nblk, 2))
    q2 = jnp.zeros_like(own)
    q2 = lax.dynamic_update_slice_in_dim(q2, c2, p * cw, axis=2)
    for m in range(1, GROUP):
        q2 = lax.dynamic_update_slice_in_dim(q2, rest[:, :, (m - 1) * cw:m * cw], (p ^ m) * cw, axis=2)
    q3 = send(q2, xor_perm(nblk, 1))
    rows = jnp.concatenate([own, q1, q2, q3], axis=1)

    l5 = rows.reshape(2, gw, ny, GROUP, rb)
    lx = jnp.concatenate(
        [lax.dynamic_slice_in_dim(l5, p ^ m, 1, axis=3) for m in range(GROUP)], axis=3
    ).reshape(2, gw, n)

    def contrib(g, pc, lo, hi):
        lg = lax.dynamic_slice_in_dim(lx, g * gw + lo * rb, (hi - lo) * rb, axis=2)
        return jnp.einsum(
            "aik,bkj->abij", lg, pc,
            precision=lax.Precision.HIGH, preferred_element_type=jnp.float32,
        )

    part_a = jnp.concatenate([cols(own, p), cols(q1, p)], axis=1)
    part_b = jnp.concatenate([c2, c3], axis=1)
    up = shift_perm(nblk, GROUP)
    dn = shift_perm(nblk, -GROUP)
    ua = send(part_a, up)
    da = send(part_a, dn)
    ub = send(part_b, up)
    db = send(part_b, dn)
    fa = send(ua, up)
    fb = send(db, dn)

    half = GROUP // 2
    t = contrib(y, part_a, 0, half) + contrib(y, part_b, half, GROUP)
    t = t + contrib((y - 1) % ny, ua, 0, half) + contrib((y + 1) % ny, da, 0, half)
    t = t + contrib((y - 1) % ny, ub, half, GROUP) + contrib((y + 1) % ny, db, half, GROUP)
    t = t + contrib((y + 2) % ny, fa, 0, half) + contrib((y + 2) % ny, fb, half, GROUP)

    prod_re = t[0, 0] - t[1, 1]
    prod_im = t[0, 1] + t[1, 0]
    scale = 1.0 / math.sqrt(n)
    w_re = signature[0, 0]
    w_im = signature[0, 1]
    out_re = -(w_re * prod_re - w_im * prod_im) * scale
    out_im = -(w_re * prod_im + w_im * prod_re) * scale
    blk_out = jnp.stack([out_re, out_im], axis=0)

    parts = [blk_out[:, :rb]]
    for m in range(1, GROUP):
        parts.append(send(blk_out[:, m * rb:(m + 1) * rb], xor_perm(nblk, m)))
    stacked = jnp.stack(parts, axis=0)
    ordered = [lax.dynamic_index_in_dim(stacked, p ^ i, 0, keepdims=False) for i in range(GROUP)]
    out = jnp.concatenate(ordered, axis=2)
    return out[None]


def solution(mesh):
    return jax.shard_map(
        on_device,
        mesh=mesh,
        in_specs=(P("blk", "freq", None), P("freq", None)),
        out_specs=P("freq", None, "blk", None),
        check_vma=False,
    )
```

```python
import math

import jax
import jax.numpy as jnp
from jax import lax
from jax.sharding import PartitionSpec as P


BIN0 = 4
BINSTEP = 3
GROUP = 4


def make_table(freqs, samples):
    bins = BIN0 + BINSTEP * jnp.arange(freqs, dtype=jnp.int32)
    steps = jnp.arange(samples, dtype=jnp.int32)
    phase = steps[:, None] * bins[None, :] % samples
    angle = phase.astype(jnp.float32) * (2.0 * math.pi / samples)
    scale = 1.0 / math.sqrt(samples)
    table = jnp.concatenate([jnp.cos(angle) * scale, -jnp.sin(angle) * scale], axis=1)
    return table.astype(jnp.bfloat16)


def xor_perm(n, m):
    return [(i, i ^ m) for i in range(n)]


def shift_perm(n, s):
    return [(i, (i + s) % n) for i in range(n)]


def send(x, perm):
    return lax.ppermute(x, "blk", perm)


def on_device(traces, signature):
    src_rows, rec_cols, samples = traces.shape
    freqs = lax.axis_size("freq")
    nblk = lax.axis_size("blk")
    ny = nblk // GROUP
    assert ny == 4 and nblk % GROUP == 0
    table = make_table(freqs, samples)
    projected = jnp.einsum("srt,tc->csr", traces, table, preferred_element_type=jnp.float32)
    projected = projected.reshape(2, freqs, src_rows, rec_cols)
    spectra = lax.all_to_all(projected, "freq", split_axis=1, concat_axis=3, tiled=True)
    own = spectra[:, 0]
    n = own.shape[2]
    rb = src_rows
    gw = GROUP * rb
    cw = n // GROUP

    b = lax.axis_index("blk")
    p = b % GROUP
    y = b // GROUP

    def cols(x, i):
        return lax.dynamic_slice_in_dim(x, i * cw, cw, axis=2)

    q1 = send(own, xor_perm(nblk, 1))
    c2 = send(cols(own, p ^ 2), xor_perm(nblk, 2))
    c3 = send(cols(own, p ^ 3), xor_perm(nblk, 3))
    rest = jnp.concatenate([cols(own, p ^ 2 ^ m) for m in range(1, GROUP)], axis=2)
    rest, _, _ = lax.optimization_barrier((rest, c2, c3))
    rest = send(rest, xor_perm(nblk, 2))
    q2 = jnp.zeros_like(own)
    q2 = lax.dynamic_update_slice_in_dim(q2, c2, p * cw, axis=2)
    for m in range(1, GROUP):
        q2 = lax.dynamic_update_slice_in_dim(q2, rest[:, :, (m - 1) * cw:m * cw], (p ^ m) * cw, axis=2)
    q3 = send(q2, xor_perm(nblk, 1))

    def reorder(r):
        l5 = r.reshape(2, r.shape[1], ny, GROUP, rb)
        return jnp.concatenate(
            [lax.dynamic_slice_in_dim(l5, p ^ m, 1, axis=3) for m in range(GROUP)], axis=3
        ).reshape(2, r.shape[1], n)

    def mm(lhs, rhs):
        return jnp.einsum(
            "aik,bkj->abij", lhs, rhs,
            precision=lax.Precision.HIGH, preferred_element_type=jnp.float32,
        )

    part_a = jnp.concatenate([cols(own, p), cols(q1, p)], axis=1)
    part_b = jnp.concatenate([c2, c3], axis=1)
    up = shift_perm(nblk, GROUP)
    dn = shift_perm(nblk, -GROUP)
    ua = send(part_a, up)
    da = send(part_a, dn)
    ub = send(part_b, up)
    db = send(part_b, dn)
    fa = send(ua, up)
    fb = send(db, dn)

    half = GROUP // 2
    hk = half * rb
    pieces = [
        (y, 0, part_a), (y, 1, part_b),
        ((y - 1) % ny, 0, ua), ((y + 1) % ny, 0, da),
        ((y - 1) % ny, 1, ub), ((y + 1) % ny, 1, db),
        ((y + 2) % ny, 0, fa), ((y + 2) % ny, 1, fb),
    ]

    early = reorder(jnp.concatenate([own, q1], axis=1))
    t_early = None
    for g, h, pc in pieces:
        lhs = lax.dynamic_slice_in_dim(early, g * gw + h * hk, hk, axis=2)
        term = mm(lhs, pc)
        t_early = term if t_early is None else t_early + term

    right = jnp.zeros((2, n, cw), jnp.float32)
    for g, h, pc in pieces:
        right = lax.dynamic_update_slice_in_dim(right, pc, g * gw + h * hk, axis=1)
    late = reorder(jnp.concatenate([q2, q3], axis=1))
    t_late = mm(late, right)
    t = jnp.concatenate([t_early, t_late], axis=2)

    prod_re = t[0, 0] - t[1, 1]
    prod_im = t[0, 1] + t[1, 0]
    scale = 1.0 / math.sqrt(n)
    w_re = signature[0, 0]
    w_im = signature[0, 1]
    out_re = -(w_re * prod_re - w_im * prod_im) * scale
    out_im = -(w_re * prod_im + w_im * prod_re) * scale
    blk_out = jnp.stack([out_re, out_im], axis=0)

    parts = [blk_out[:, :rb]]
    for m in range(1, GROUP):
        parts.append(send(blk_out[:, m * rb:(m + 1) * rb], xor_perm(nblk, m)))
    stacked = jnp.stack(parts, axis=0)
    ordered = [lax.dynamic_index_in_dim(stacked, p ^ i, 0, keepdims=False) for i in range(GROUP)]
    out = jnp.concatenate(ordered, axis=2)
    return out[None]


def solution(mesh):
    return jax.shard_map(
        on_device,
        mesh=mesh,
        in_specs=(P("blk", "freq", None), P("freq", None)),
        out_specs=P("freq", None, "blk", None),
        check_vma=False,
    )
```

```python
import math

import jax
import jax.numpy as jnp
from jax import lax
from jax.sharding import PartitionSpec as P


BIN0 = 4
BINSTEP = 3
GROUP = 4


def make_table(freqs, samples):
    bins = BIN0 + BINSTEP * jnp.arange(freqs, dtype=jnp.int32)
    steps = jnp.arange(samples, dtype=jnp.int32)
    phase = steps[:, None] * bins[None, :] % samples
    angle = phase.astype(jnp.float32) * (2.0 * math.pi / samples)
    scale = 1.0 / math.sqrt(samples)
    table = jnp.concatenate([jnp.cos(angle) * scale, -jnp.sin(angle) * scale], axis=1)
    return table.astype(jnp.bfloat16)


def xor_perm(n, m):
    return [(i, i ^ m) for i in range(n)]


def shift_perm(n, s):
    return [(i, (i + s) % n) for i in range(n)]


def send(x, perm):
    return lax.ppermute(x, "blk", perm)


def on_device(traces, signature):
    src_rows, rec_cols, samples = traces.shape
    freqs = lax.axis_size("freq")
    nblk = lax.axis_size("blk")
    ny = nblk // GROUP
    assert ny == 4 and nblk % GROUP == 0
    table = make_table(freqs, samples)
    projected = jnp.einsum("srt,tc->csr", traces, table, preferred_element_type=jnp.float32)
    projected = projected.reshape(2, freqs, src_rows, rec_cols)
    spectra = lax.all_to_all(projected, "freq", split_axis=1, concat_axis=3, tiled=True)
    own = spectra[:, 0]
    n = own.shape[2]
    rb = src_rows
    cw = n // GROUP

    b = lax.axis_index("blk")
    p = b % GROUP
    y = b // GROUP

    def cols(x, i):
        return lax.dynamic_slice_in_dim(x, i * cw, cw, axis=2)

    q1 = send(own, xor_perm(nblk, 1))
    c2 = send(cols(own, p ^ 2), xor_perm(nblk, 2))
    c3 = send(cols(own, p ^ 3), xor_perm(nblk, 3))
    rest = jnp.concatenate([cols(own, p ^ 2 ^ m) for m in range(1, GROUP)], axis=2)
    rest, _, _ = lax.optimization_barrier((rest, c2, c3))
    rest = send(rest, xor_perm(nblk, 2))
    q2 = jnp.zeros_like(own)
    q2 = lax.dynamic_update_slice_in_dim(q2, c2, p * cw, axis=2)
    for m in range(1, GROUP):
        q2 = lax.dynamic_update_slice_in_dim(q2, rest[:, :, (m - 1) * cw:m * cw], (p ^ m) * cw, axis=2)
    q3 = send(q2, xor_perm(nblk, 1))

    def mm(lhs, rhs):
        return jnp.einsum(
            "aik,bkj->abij", lhs, rhs,
            precision=lax.Precision.HIGH, preferred_element_type=jnp.float32,
        )

    part_a = jnp.concatenate([cols(own, p), cols(q1, p)], axis=1)
    part_b = jnp.concatenate([c2, c3], axis=1)
    up = shift_perm(nblk, GROUP)
    dn = shift_perm(nblk, -GROUP)
    ua = send(part_a, up)
    da = send(part_a, dn)
    ub = send(part_b, up)
    db = send(part_b, dn)
    fa = send(ua, up)
    fb = send(db, dn)

    half = GROUP // 2
    pieces = [
        (y, 0, part_a), (y, 1, part_b),
        ((y - 1) % ny, 0, ua), ((y + 1) % ny, 0, da),
        ((y - 1) % ny, 1, ub), ((y + 1) % ny, 1, db),
        ((y + 2) % ny, 0, fa), ((y + 2) % ny, 1, fb),
    ]

    def kblk(g, m):
        return (GROUP * g + (p ^ m)) * rb

    early = jnp.concatenate([own, q1], axis=1)
    t_early = None
    for g, h, pc in pieces:
        lhs = jnp.concatenate(
            [lax.dynamic_slice_in_dim(early, kblk(g, half * h + i), rb, axis=2) for i in range(half)],
            axis=2,
        )
        term = mm(lhs, pc)
        t_early = term if t_early is None else t_early + term

    right = jnp.zeros((2, n, cw), jnp.float32)
    for g, h, pc in pieces:
        for i in range(half):
            right = lax.dynamic_update_slice_in_dim(
                right, pc[:, i * rb:(i + 1) * rb], kblk(g, half * h + i), axis=1
            )
    late = jnp.concatenate([q2, q3], axis=1)
    t_late = mm(late, right)
    t = jnp.concatenate([t_early, t_late], axis=2)

    prod_re = t[0, 0] - t[1, 1]
    prod_im = t[0, 1] + t[1, 0]
    scale = 1.0 / math.sqrt(n)
    w_re = signature[0, 0]
    w_im = signature[0, 1]
    out_re = -(w_re * prod_re - w_im * prod_im) * scale
    out_im = -(w_re * prod_im + w_im * prod_re) * scale
    blk_out = jnp.stack([out_re, out_im], axis=0)

    parts = [blk_out[:, :rb]]
    for m in range(1, GROUP):
        parts.append(send(blk_out[:, m * rb:(m + 1) * rb], xor_perm(nblk, m)))
    stacked = jnp.stack(parts, axis=0)
    ordered = [lax.dynamic_index_in_dim(stacked, p ^ i, 0, keepdims=False) for i in range(GROUP)]
    out = jnp.concatenate(ordered, axis=2)
    return out[None]


def solution(mesh):
    return jax.shard_map(
        on_device,
        mesh=mesh,
        in_specs=(P("blk", "freq", None), P("freq", None)),
        out_specs=P("freq", None, "blk", None),
        check_vma=False,
    )
```

```python
import math

import jax
import jax.numpy as jnp
from jax import lax
from jax.sharding import PartitionSpec as P


BIN0 = 4
BINSTEP = 3
GROUP = 4


def make_table(freqs, samples):
    bins = BIN0 + BINSTEP * jnp.arange(freqs, dtype=jnp.int32)
    steps = jnp.arange(samples, dtype=jnp.int32)
    phase = steps[:, None] * bins[None, :] % samples
    angle = phase.astype(jnp.float32) * (2.0 * math.pi / samples)
    scale = 1.0 / math.sqrt(samples)
    table = jnp.concatenate([jnp.cos(angle) * scale, -jnp.sin(angle) * scale], axis=1)
    return table.astype(jnp.bfloat16)


def xor_perm(n, m):
    return [(i, i ^ m) for i in range(n)]


def shift_perm(n, s):
    return [(i, (i + s) % n) for i in range(n)]


def send(x, perm):
    return lax.ppermute(x, "blk", perm)


def on_device(traces, signature):
    src_rows, rec_cols, samples = traces.shape
    freqs = lax.axis_size("freq")
    nblk = lax.axis_size("blk")
    ny = nblk // GROUP
    assert ny == 4 and nblk % GROUP == 0
    table = make_table(freqs, samples)
    projected = jnp.einsum("srt,tc->csr", traces, table, preferred_element_type=jnp.float32)
    projected = projected.reshape(2, freqs, src_rows, rec_cols)
    spectra = lax.all_to_all(projected, "freq", split_axis=1, concat_axis=3, tiled=True)
    own = spectra[:, 0]
    n = own.shape[2]
    rb = src_rows
    cw = n // GROUP

    b = lax.axis_index("blk")
    p = b % GROUP
    y = b // GROUP

    def cols(x, i):
        return lax.dynamic_slice_in_dim(x, i * cw, cw, axis=2)

    q1 = send(own, xor_perm(nblk, 1))
    c2 = send(cols(own, p ^ 2), xor_perm(nblk, 2))
    c3 = send(cols(own, p ^ 3), xor_perm(nblk, 3))
    rest = jnp.concatenate([cols(own, p), cols(own, p ^ 1)], axis=2)
    rest, _, _ = lax.optimization_barrier((rest, c2, c3))
    rest = send(rest, xor_perm(nblk, 2))
    r_c = send(jnp.concatenate([c2, c3], axis=2), xor_perm(nblk, 1))
    r_rest = send(rest, xor_perm(nblk, 1))

    def assemble(blocks):
        out = jnp.zeros_like(own)
        for m, blk in blocks:
            out = lax.dynamic_update_slice_in_dim(out, blk, (p ^ m) * cw, axis=2)
        return out

    q2 = assemble([
        (0, c2), (1, r_c[:, :, cw:]), (2, rest[:, :, :cw]), (3, rest[:, :, cw:]),
    ])
    q3 = assemble([
        (0, c3), (1, r_c[:, :, :cw]), (3, r_rest[:, :, :cw]), (2, r_rest[:, :, cw:]),
    ])

    def mm(lhs, rhs):
        return jnp.einsum(
            "aik,bkj->abij", lhs, rhs,
            precision=lax.Precision.HIGH, preferred_element_type=jnp.float32,
        )

    part_a = jnp.concatenate([cols(own, p), cols(q1, p)], axis=1)
    part_b = jnp.concatenate([c2, c3], axis=1)
    up = shift_perm(nblk, GROUP)
    dn = shift_perm(nblk, -GROUP)
    ua = send(part_a, up)
    da = send(part_a, dn)
    ub = send(part_b, up)
    db = send(part_b, dn)
    fa = send(ua, up)
    fb = send(db, dn)

    half = GROUP // 2
    pieces = [
        (y, 0, part_a), (y, 1, part_b),
        ((y - 1) % ny, 0, ua), ((y + 1) % ny, 0, da),
        ((y - 1) % ny, 1, ub), ((y + 1) % ny, 1, db),
        ((y + 2) % ny, 0, fa), ((y + 2) % ny, 1, fb),
    ]

    def kblk(g, m):
        return (GROUP * g + (p ^ m)) * rb

    early = jnp.concatenate([own, q1], axis=1)
    t_early = None
    for g, h, pc in pieces:
        lhs = jnp.concatenate(
            [lax.dynamic_slice_in_dim(early, kblk(g, half * h + i), rb, axis=2) for i in range(half)],
            axis=2,
        )
        term = mm(lhs, pc)
        t_early = term if t_early is None else t_early + term

    right = jnp.zeros((2, n, cw), jnp.float32)
    for g, h, pc in pieces:
        for i in range(half):
            right = lax.dynamic_update_slice_in_dim(
                right, pc[:, i * rb:(i + 1) * rb], kblk(g, half * h + i), axis=1
            )
    scale = 1.0 / math.sqrt(n)
    w_re = signature[0, 0]
    w_im = signature[0, 1]

    def finish(t):
        prod_re = t[0, 0] - t[1, 1]
        prod_im = t[0, 1] + t[1, 0]
        out_re = -(w_re * prod_re - w_im * prod_im) * scale
        out_im = -(w_re * prod_im + w_im * prod_re) * scale
        return jnp.stack([out_re, out_im], axis=0)

    out_early = finish(t_early)
    out_2 = send(finish(mm(q2, right)), xor_perm(nblk, 2))
    out_3 = send(finish(mm(q3, right)), xor_perm(nblk, 3))
    out_1 = send(out_early[:, rb:], xor_perm(nblk, 1))

    stacked = jnp.stack([out_early[:, :rb], out_1, out_2, out_3], axis=0)
    ordered = [lax.dynamic_index_in_dim(stacked, p ^ i, 0, keepdims=False) for i in range(GROUP)]
    out = jnp.concatenate(ordered, axis=2)
    return out[None]


def solution(mesh):
    return jax.shard_map(
        on_device,
        mesh=mesh,
        in_specs=(P("blk", "freq", None), P("freq", None)),
        out_specs=P("freq", None, "blk", None),
        check_vma=False,
    )
```

```python
import math

import jax
import jax.numpy as jnp
from jax import lax
from jax.sharding import PartitionSpec as P


BIN0 = 4
BINSTEP = 3
GROUP = 4


def make_table(freqs, samples):
    bins = BIN0 + BINSTEP * jnp.arange(freqs, dtype=jnp.int32)
    steps = jnp.arange(samples, dtype=jnp.int32)
    phase = steps[:, None] * bins[None, :] % samples
    angle = phase.astype(jnp.float32) * (2.0 * math.pi / samples)
    scale = 1.0 / math.sqrt(samples)
    table = jnp.concatenate([jnp.cos(angle) * scale, -jnp.sin(angle) * scale], axis=1)
    return table.astype(jnp.bfloat16)


def xor_perm(n, m):
    return [(i, i ^ m) for i in range(n)]


def shift_perm(n, s):
    return [(i, (i + s) % n) for i in range(n)]


def send(x, perm):
    return lax.ppermute(x, "blk", perm)


def on_device(traces, signature):
    src_rows, rec_cols, samples = traces.shape
    freqs = lax.axis_size("freq")
    nblk = lax.axis_size("blk")
    ny = nblk // GROUP
    assert ny == 4 and nblk % GROUP == 0
    table = make_table(freqs, samples)
    projected = jnp.einsum("srt,tc->csr", traces, table, preferred_element_type=jnp.float32)
    projected = projected.reshape(2, freqs, src_rows, rec_cols)
    spectra = lax.all_to_all(projected, "freq", split_axis=1, concat_axis=3, tiled=True)
    own = spectra[:, 0]
    n = own.shape[2]
    rb = src_rows
    cw = n // GROUP

    b = lax.axis_index("blk")
    p = b % GROUP
    y = b // GROUP

    def cols(x, i):
        return lax.dynamic_slice_in_dim(x, i * cw, cw, axis=2)

    q1 = send(own, xor_perm(nblk, 1))
    c2 = send(cols(own, p ^ 2), xor_perm(nblk, 2))
    c3 = send(cols(own, p ^ 3), xor_perm(nblk, 3))
    rest = jnp.concatenate([cols(own, p), cols(own, p ^ 1)], axis=2)
    rest, _, _ = lax.optimization_barrier((rest, c2, c3))
    rest = send(rest, xor_perm(nblk, 2))
    r_c = send(jnp.concatenate([c2, c3], axis=2), xor_perm(nblk, 1))
    r_rest = send(rest, xor_perm(nblk, 1))

    def assemble(blocks):
        out = jnp.zeros_like(own)
        for m, blk in blocks:
            out = lax.dynamic_update_slice_in_dim(out, blk, (p ^ m) * cw, axis=2)
        return out

    q2 = assemble([
        (0, c2), (1, r_c[:, :, cw:]), (2, rest[:, :, :cw]), (3, rest[:, :, cw:]),
    ])
    q3 = assemble([
        (0, c3), (1, r_c[:, :, :cw]), (3, r_rest[:, :, :cw]), (2, r_rest[:, :, cw:]),
    ])

    def mm(lhs, rhs):
        return jnp.einsum(
            "aik,bkj->abij", lhs, rhs,
            precision=lax.Precision.HIGH, preferred_element_type=jnp.float32,
        )

    part_a = jnp.concatenate([cols(own, p), cols(q1, p)], axis=1)
    part_b = jnp.concatenate([c2, c3], axis=1)
    up = shift_perm(nblk, GROUP)
    dn = shift_perm(nblk, -GROUP)
    ua = send(part_a, up)
    da = send(part_a, dn)
    ub = send(part_b, up)
    db = send(part_b, dn)
    fa = send(ua, up)
    fb = send(db, dn)

    half = GROUP // 2
    pieces = [
        (y, 0, part_a), (y, 1, part_b),
        ((y - 1) % ny, 0, ua), ((y + 1) % ny, 0, da),
        ((y - 1) % ny, 1, ub), ((y + 1) % ny, 1, db),
        ((y + 2) % ny, 0, fa), ((y + 2) % ny, 1, fb),
    ]

    def kblk(g, m):
        return (GROUP * g + (p ^ m)) * rb

    early = jnp.concatenate([own, q1], axis=1)
    t_early = None
    for g, h, pc in pieces:
        lhs = jnp.concatenate(
            [lax.dynamic_slice_in_dim(early, kblk(g, half * h + i), rb, axis=2) for i in range(half)],
            axis=2,
        )
        term = mm(lhs, pc)
        t_early = term if t_early is None else t_early + term

    right = jnp.zeros((2, n, cw), jnp.float32)
    for g, h, pc in pieces:
        for i in range(half):
            right = lax.dynamic_update_slice_in_dim(
                right, pc[:, i * rb:(i + 1) * rb], kblk(g, half * h + i), axis=1
            )
    late = jnp.concatenate([q2, q3], axis=1)
    t_late = mm(late, right)
    t = jnp.concatenate([t_early, t_late], axis=2)

    prod_re = t[0, 0] - t[1, 1]
    prod_im = t[0, 1] + t[1, 0]
    scale = 1.0 / math.sqrt(n)
    w_re = signature[0, 0]
    w_im = signature[0, 1]
    out_re = -(w_re * prod_re - w_im * prod_im) * scale
    out_im = -(w_re * prod_im + w_im * prod_re) * scale
    blk_out = jnp.stack([out_re, out_im], axis=0)

    parts = [blk_out[:, :rb]]
    for m in range(1, GROUP):
        parts.append(send(blk_out[:, m * rb:(m + 1) * rb], xor_perm(nblk, m)))
    stacked = jnp.stack(parts, axis=0)
    ordered = [lax.dynamic_index_in_dim(stacked, p ^ i, 0, keepdims=False) for i in range(GROUP)]
    out = jnp.concatenate(ordered, axis=2)
    return out[None]


def solution(mesh):
    return jax.shard_map(
        on_device,
        mesh=mesh,
        in_specs=(P("blk", "freq", None), P("freq", None)),
        out_specs=P("freq", None, "blk", None),
        check_vma=False,
    )
```

```python
import math

import jax
import jax.numpy as jnp
from jax import lax
from jax.sharding import PartitionSpec as P


BIN0 = 4
BINSTEP = 3
GROUP = 4


def make_table(freqs, samples):
    bins = BIN0 + BINSTEP * jnp.arange(freqs, dtype=jnp.int32)
    steps = jnp.arange(samples, dtype=jnp.int32)
    phase = steps[:, None] * bins[None, :] % samples
    angle = phase.astype(jnp.float32) * (2.0 * math.pi / samples)
    scale = 1.0 / math.sqrt(samples)
    table = jnp.concatenate([jnp.cos(angle) * scale, -jnp.sin(angle) * scale], axis=1)
    return table.astype(jnp.bfloat16)


def xor_perm(n, m):
    return [(i, i ^ m) for i in range(n)]


def shift_perm(n, s):
    return [(i, (i + s) % n) for i in range(n)]


def send(x, perm):
    return lax.ppermute(x, "blk", perm)


def on_device(traces, signature):
    src_rows, rec_cols, samples = traces.shape
    freqs = lax.axis_size("freq")
    nblk = lax.axis_size("blk")
    ny = nblk // GROUP
    assert ny == 4 and nblk % GROUP == 0
    table = make_table(freqs, samples)
    projected = jnp.einsum("srt,tc->csr", traces, table, preferred_element_type=jnp.float32)
    projected = projected.reshape(2, freqs, src_rows, rec_cols)
    spectra = lax.all_to_all(projected, "freq", split_axis=1, concat_axis=3, tiled=True)
    own = spectra[:, 0]
    n = own.shape[2]
    rb = src_rows
    cw = n // GROUP

    b = lax.axis_index("blk")
    p = b % GROUP
    y = b // GROUP

    def cols(x, i):
        return lax.dynamic_slice_in_dim(x, i * cw, cw, axis=2)

    q1 = send(own, xor_perm(nblk, 1))
    c2 = send(cols(own, p ^ 2), xor_perm(nblk, 2))
    c3 = send(cols(own, p ^ 3), xor_perm(nblk, 3))
    rest = jnp.concatenate([cols(own, p), cols(own, p ^ 1)], axis=2)
    rest, _, _ = lax.optimization_barrier((rest, c2, c3))
    rest = send(rest, xor_perm(nblk, 2))
    r_c = send(jnp.concatenate([c2, c3], axis=2), xor_perm(nblk, 1))
    r_rest = send(rest, xor_perm(nblk, 1))

    def assemble(blocks):
        out = jnp.zeros_like(own)
        for m, blk in blocks:
            out = lax.dynamic_update_slice_in_dim(out, blk, (p ^ m) * cw, axis=2)
        return out

    q2 = assemble([
        (0, c2), (1, r_c[:, :, cw:]), (2, rest[:, :, :cw]), (3, rest[:, :, cw:]),
    ])
    q3 = assemble([
        (0, c3), (1, r_c[:, :, :cw]), (3, r_rest[:, :, :cw]), (2, r_rest[:, :, cw:]),
    ])

    def mm(lhs, rhs):
        return jnp.einsum(
            "aik,bkj->abij", lhs, rhs,
            precision=lax.Precision.HIGH, preferred_element_type=jnp.float32,
        )

    part_a = jnp.concatenate([cols(own, p), cols(q1, p)], axis=1)
    part_b = jnp.concatenate([c2, c3], axis=1)
    up = shift_perm(nblk, GROUP)
    dn = shift_perm(nblk, -GROUP)
    ua = send(part_a, up)
    da = send(part_a, dn)
    ub = send(part_b, up)
    db = send(part_b, dn)
    fa0 = send(ua[:, :rb], up)
    fa1 = send(da[:, rb:], dn)
    fb0 = send(ub[:, :rb], up)
    fb1 = send(db[:, rb:], dn)

    pieces = [
        (y, (0, 1), part_a), (y, (2, 3), part_b),
        ((y - 1) % ny, (0, 1), ua), ((y + 1) % ny, (0, 1), da),
        ((y - 1) % ny, (2, 3), ub), ((y + 1) % ny, (2, 3), db),
        ((y + 2) % ny, (0,), fa0), ((y + 2) % ny, (1,), fa1),
        ((y + 2) % ny, (2,), fb0), ((y + 2) % ny, (3,), fb1),
    ]

    def kblk(g, m):
        return (GROUP * g + (p ^ m)) * rb

    early = jnp.concatenate([own, q1], axis=1)
    t_early = None
    for g, ms, pc in pieces:
        lhs = jnp.concatenate(
            [lax.dynamic_slice_in_dim(early, kblk(g, m), rb, axis=2) for m in ms], axis=2
        )
        term = mm(lhs, pc)
        t_early = term if t_early is None else t_early + term

    right = jnp.zeros((2, n, cw), jnp.float32)
    for g, ms, pc in pieces:
        for i, m in enumerate(ms):
            right = lax.dynamic_update_slice_in_dim(
                right, pc[:, i * rb:(i + 1) * rb], kblk(g, m), axis=1
            )
    late = jnp.concatenate([q2, q3], axis=1)
    t_late = mm(late, right)
    t = jnp.concatenate([t_early, t_late], axis=2)

    prod_re = t[0, 0] - t[1, 1]
    prod_im = t[0, 1] + t[1, 0]
    scale = 1.0 / math.sqrt(n)
    w_re = signature[0, 0]
    w_im = signature[0, 1]
    out_re = -(w_re * prod_re - w_im * prod_im) * scale
    out_im = -(w_re * prod_im + w_im * prod_re) * scale
    blk_out = jnp.stack([out_re, out_im], axis=0)

    parts = [blk_out[:, :rb]]
    for m in range(1, GROUP):
        parts.append(send(blk_out[:, m * rb:(m + 1) * rb], xor_perm(nblk, m)))
    stacked = jnp.stack(parts, axis=0)
    ordered = [lax.dynamic_index_in_dim(stacked, p ^ i, 0, keepdims=False) for i in range(GROUP)]
    out = jnp.concatenate(ordered, axis=2)
    return out[None]


def solution(mesh):
    return jax.shard_map(
        on_device,
        mesh=mesh,
        in_specs=(P("blk", "freq", None), P("freq", None)),
        out_specs=P("freq", None, "blk", None),
        check_vma=False,
    )
```

```python
import math

import jax
import jax.numpy as jnp
from jax import lax
from jax.sharding import PartitionSpec as P


BIN0 = 4
BINSTEP = 3
GROUP = 4


def make_table(freqs, samples):
    bins = BIN0 + BINSTEP * jnp.arange(freqs, dtype=jnp.int32)
    steps = jnp.arange(samples, dtype=jnp.int32)
    phase = steps[:, None] * bins[None, :] % samples
    angle = phase.astype(jnp.float32) * (2.0 * math.pi / samples)
    scale = 1.0 / math.sqrt(samples)
    table = jnp.concatenate([jnp.cos(angle) * scale, -jnp.sin(angle) * scale], axis=1)
    return table.astype(jnp.bfloat16)


def xor_perm(n, m):
    return [(i, i ^ m) for i in range(n)]


def shift_perm(n, s):
    return [(i, (i + s) % n) for i in range(n)]


def send(x, perm):
    return lax.ppermute(x, "blk", perm)


def on_device(traces, signature):
    src_rows, rec_cols, samples = traces.shape
    freqs = lax.axis_size("freq")
    nblk = lax.axis_size("blk")
    ny = nblk // GROUP
    assert ny == 4 and nblk % GROUP == 0
    table = make_table(freqs, samples)
    table = table.reshape(samples, 2, freqs).transpose(0, 2, 1).reshape(samples, 2 * freqs)
    projected = jnp.einsum("srt,tc->csr", traces, table, preferred_element_type=jnp.float32)
    projected = projected.reshape(freqs, 2, src_rows, rec_cols)
    spectra = lax.all_to_all(projected, "freq", split_axis=0, concat_axis=3, tiled=True)
    own = spectra[0]
    n = own.shape[2]
    rb = src_rows
    cw = n // GROUP

    b = lax.axis_index("blk")
    p = b % GROUP
    y = b // GROUP

    def cols(x, i):
        return lax.dynamic_slice_in_dim(x, i * cw, cw, axis=2)

    q1 = send(own, xor_perm(nblk, 1))
    c2 = send(cols(own, p ^ 2), xor_perm(nblk, 2))
    c3 = send(cols(own, p ^ 3), xor_perm(nblk, 3))
    rest = jnp.concatenate([cols(own, p ^ 2 ^ m) for m in range(1, GROUP)], axis=2)
    rest, _, _ = lax.optimization_barrier((rest, c2, c3))
    rest = send(rest, xor_perm(nblk, 2))
    q2 = jnp.zeros_like(own)
    q2 = lax.dynamic_update_slice_in_dim(q2, c2, p * cw, axis=2)
    for m in range(1, GROUP):
        q2 = lax.dynamic_update_slice_in_dim(q2, rest[:, :, (m - 1) * cw:m * cw], (p ^ m) * cw, axis=2)
    q3 = send(q2, xor_perm(nblk, 1))

    def mm(lhs, rhs):
        return jnp.einsum(
            "aik,bkj->abij", lhs, rhs,
            precision=lax.Precision.HIGH, preferred_element_type=jnp.float32,
        )

    part_a = jnp.concatenate([cols(own, p), cols(q1, p)], axis=1)
    part_b = jnp.concatenate([c2, c3], axis=1)
    up = shift_perm(nblk, GROUP)
    dn = shift_perm(nblk, -GROUP)
    ua = send(part_a, up)
    da = send(part_a, dn)
    ub = send(part_b, up)
    db = send(part_b, dn)
    fa = send(ua, up)
    fb = send(db, dn)

    half = GROUP // 2
    pieces = [
        (y, 0, part_a), (y, 1, part_b),
        ((y - 1) % ny, 0, ua), ((y + 1) % ny, 0, da),
        ((y - 1) % ny, 1, ub), ((y + 1) % ny, 1, db),
        ((y + 2) % ny, 0, fa), ((y + 2) % ny, 1, fb),
    ]

    def kblk(g, m):
        return (GROUP * g + (p ^ m)) * rb

    early = jnp.concatenate([own, q1], axis=1)
    t_early = None
    for g, h, pc in pieces:
        lhs = jnp.concatenate(
            [lax.dynamic_slice_in_dim(early, kblk(g, half * h + i), rb, axis=2) for i in range(half)],
            axis=2,
        )
        term = mm(lhs, pc)
        t_early = term if t_early is None else t_early + term

    right = jnp.zeros((2, n, cw), jnp.float32)
    for g, h, pc in pieces:
        for i in range(half):
            right = lax.dynamic_update_slice_in_dim(
                right, pc[:, i * rb:(i + 1) * rb], kblk(g, half * h + i), axis=1
            )
    late = jnp.concatenate([q2, q3], axis=1)
    t_late = mm(late, right)
    t = jnp.concatenate([t_early, t_late], axis=2)

    prod_re = t[0, 0] - t[1, 1]
    prod_im = t[0, 1] + t[1, 0]
    scale = 1.0 / math.sqrt(n)
    w_re = signature[0, 0]
    w_im = signature[0, 1]
    out_re = -(w_re * prod_re - w_im * prod_im) * scale
    out_im = -(w_re * prod_im + w_im * prod_re) * scale
    blk_out = jnp.stack([out_re, out_im], axis=0)

    parts = [blk_out[:, :rb]]
    for m in range(1, GROUP):
        parts.append(send(blk_out[:, m * rb:(m + 1) * rb], xor_perm(nblk, m)))
    stacked = jnp.stack(parts, axis=0)
    ordered = [lax.dynamic_index_in_dim(stacked, p ^ i, 0, keepdims=False) for i in range(GROUP)]
    out = jnp.concatenate(ordered, axis=2)
    return out[None]


def solution(mesh):
    return jax.shard_map(
        on_device,
        mesh=mesh,
        in_specs=(P("blk", "freq", None), P("freq", None)),
        out_specs=P("freq", None, "blk", None),
        check_vma=False,
    )
```

```python
import math

import jax
import jax.numpy as jnp
from jax import lax
from jax.sharding import PartitionSpec as P


BIN0 = 4
BINSTEP = 3
GROUP = 4


def make_table(freqs, samples):
    bins = BIN0 + BINSTEP * jnp.arange(freqs, dtype=jnp.int32)
    steps = jnp.arange(samples, dtype=jnp.int32)
    phase = steps[:, None] * bins[None, :] % samples
    angle = phase.astype(jnp.float32) * (2.0 * math.pi / samples)
    scale = 1.0 / math.sqrt(samples)
    table = jnp.concatenate([jnp.cos(angle) * scale, -jnp.sin(angle) * scale], axis=1)
    return table.astype(jnp.bfloat16)


def xor_perm(n, m):
    return [(i, i ^ m) for i in range(n)]


def shift_perm(n, s):
    return [(i, (i + s) % n) for i in range(n)]


def send(x, perm):
    return lax.ppermute(x, "blk", perm)


def on_device(traces, signature):
    src_rows, rec_cols, samples = traces.shape
    freqs = lax.axis_size("freq")
    nblk = lax.axis_size("blk")
    ny = nblk // GROUP
    assert ny == 4 and nblk % GROUP == 0
    table = make_table(freqs, samples)
    table = table.reshape(samples, 2, freqs).transpose(0, 2, 1).reshape(samples, 2 * freqs)
    projected = jnp.einsum("srt,tc->csr", traces, table, preferred_element_type=jnp.float32)
    projected = projected.reshape(freqs, 2, src_rows, rec_cols)
    f = lax.axis_index("freq")
    own = jnp.zeros((2, src_rows, freqs * rec_cols), jnp.float32)
    own = lax.dynamic_update_slice_in_dim(
        own, lax.dynamic_index_in_dim(projected, f, 0, keepdims=False), f * rec_cols, axis=2
    )
    for k in range(1, freqs):
        chunk = lax.dynamic_index_in_dim(projected, (f + k) % freqs, 0, keepdims=False)
        got = lax.ppermute(chunk, "freq", shift_perm(freqs, k))
        own = lax.dynamic_update_slice_in_dim(own, got, ((f - k) % freqs) * rec_cols, axis=2)
    n = own.shape[2]
    rb = src_rows
    cw = n // GROUP

    b = lax.axis_index("blk")
    p = b % GROUP
    y = b // GROUP

    def cols(x, i):
        return lax.dynamic_slice_in_dim(x, i * cw, cw, axis=2)

    q1 = send(own, xor_perm(nblk, 1))
    c2 = send(cols(own, p ^ 2), xor_perm(nblk, 2))
    c3 = send(cols(own, p ^ 3), xor_perm(nblk, 3))
    rest = jnp.concatenate([cols(own, p ^ 2 ^ m) for m in range(1, GROUP)], axis=2)
    rest, _, _ = lax.optimization_barrier((rest, c2, c3))
    rest = send(rest, xor_perm(nblk, 2))
    q2 = jnp.zeros_like(own)
    q2 = lax.dynamic_update_slice_in_dim(q2, c2, p * cw, axis=2)
    for m in range(1, GROUP):
        q2 = lax.dynamic_update_slice_in_dim(q2, rest[:, :, (m - 1) * cw:m * cw], (p ^ m) * cw, axis=2)
    q3 = send(q2, xor_perm(nblk, 1))

    def mm(lhs, rhs):
        return jnp.einsum(
            "aik,bkj->abij", lhs, rhs,
            precision=lax.Precision.HIGH, preferred_element_type=jnp.float32,
        )

    part_a = jnp.concatenate([cols(own, p), cols(q1, p)], axis=1)
    part_b = jnp.concatenate([c2, c3], axis=1)
    up = shift_perm(nblk, GROUP)
    dn = shift_perm(nblk, -GROUP)
    ua = send(part_a, up)
    da = send(part_a, dn)
    ub = send(part_b, up)
    db = send(part_b, dn)
    fa = send(ua, up)
    fb = send(db, dn)

    half = GROUP // 2
    pieces = [
        (y, 0, part_a), (y, 1, part_b),
        ((y - 1) % ny, 0, ua), ((y + 1) % ny, 0, da),
        ((y - 1) % ny, 1, ub), ((y + 1) % ny, 1, db),
        ((y + 2) % ny, 0, fa), ((y + 2) % ny, 1, fb),
    ]

    def kblk(g, m):
        return (GROUP * g + (p ^ m)) * rb

    early = jnp.concatenate([own, q1], axis=1)
    t_early = None
    for g, h, pc in pieces:
        lhs = jnp.concatenate(
            [lax.dynamic_slice_in_dim(early, kblk(g, half * h + i), rb, axis=2) for i in range(half)],
            axis=2,
        )
        term = mm(lhs, pc)
        t_early = term if t_early is None else t_early + term

    right = jnp.zeros((2, n, cw), jnp.float32)
    for g, h, pc in pieces:
        for i in range(half):
            right = lax.dynamic_update_slice_in_dim(
                right, pc[:, i * rb:(i + 1) * rb], kblk(g, half * h + i), axis=1
            )
    late = jnp.concatenate([q2, q3], axis=1)
    t_late = mm(late, right)
    t = jnp.concatenate([t_early, t_late], axis=2)

    prod_re = t[0, 0] - t[1, 1]
    prod_im = t[0, 1] + t[1, 0]
    scale = 1.0 / math.sqrt(n)
    w_re = signature[0, 0]
    w_im = signature[0, 1]
    out_re = -(w_re * prod_re - w_im * prod_im) * scale
    out_im = -(w_re * prod_im + w_im * prod_re) * scale
    blk_out = jnp.stack([out_re, out_im], axis=0)

    parts = [blk_out[:, :rb]]
    for m in range(1, GROUP):
        parts.append(send(blk_out[:, m * rb:(m + 1) * rb], xor_perm(nblk, m)))
    stacked = jnp.stack(parts, axis=0)
    ordered = [lax.dynamic_index_in_dim(stacked, p ^ i, 0, keepdims=False) for i in range(GROUP)]
    out = jnp.concatenate(ordered, axis=2)
    return out[None]


def solution(mesh):
    return jax.shard_map(
        on_device,
        mesh=mesh,
        in_specs=(P("blk", "freq", None), P("freq", None)),
        out_specs=P("freq", None, "blk", None),
        check_vma=False,
    )
```

```python
import math

import jax
import jax.numpy as jnp
from jax import lax
from jax.sharding import PartitionSpec as P


BIN0 = 4
BINSTEP = 3
GROUP = 4


def make_table(freqs, samples, first=0):
    bins = BIN0 + BINSTEP * ((first + jnp.arange(freqs, dtype=jnp.int32)) % freqs)
    steps = jnp.arange(samples, dtype=jnp.int32)
    phase = steps[:, None] * bins[None, :] % samples
    angle = phase.astype(jnp.float32) * (2.0 * math.pi / samples)
    scale = 1.0 / math.sqrt(samples)
    table = jnp.concatenate([jnp.cos(angle) * scale, -jnp.sin(angle) * scale], axis=1)
    return table.astype(jnp.bfloat16)


def xor_perm(n, m):
    return [(i, i ^ m) for i in range(n)]


def shift_perm(n, s):
    return [(i, (i + s) % n) for i in range(n)]


def send(x, perm):
    return lax.ppermute(x, "blk", perm)


def on_device(traces, signature):
    src_rows, rec_cols, samples = traces.shape
    freqs = lax.axis_size("freq")
    nblk = lax.axis_size("blk")
    ny = nblk // GROUP
    assert ny == 4 and nblk % GROUP == 0
    f = lax.axis_index("freq")
    table = make_table(freqs, samples, f)
    table = table.reshape(samples, 2, freqs).transpose(0, 2, 1).reshape(samples, 2 * freqs)
    projected = jnp.einsum("srt,tc->csr", traces, table, preferred_element_type=jnp.float32)
    projected = projected.reshape(freqs, 2, src_rows, rec_cols)
    own = jnp.zeros((2, src_rows, freqs * rec_cols), jnp.float32)
    own = lax.dynamic_update_slice_in_dim(own, projected[0], f * rec_cols, axis=2)
    for k in range(1, freqs):
        chunk = projected[k]
        got = lax.ppermute(chunk, "freq", shift_perm(freqs, k))
        own = lax.dynamic_update_slice_in_dim(own, got, ((f - k) % freqs) * rec_cols, axis=2)
    n = own.shape[2]
    rb = src_rows
    cw = n // GROUP

    b = lax.axis_index("blk")
    p = b % GROUP
    y = b // GROUP

    def cols(x, i):
        return lax.dynamic_slice_in_dim(x, i * cw, cw, axis=2)

    q1 = send(own, xor_perm(nblk, 1))
    c2 = send(cols(own, p ^ 2), xor_perm(nblk, 2))
    c3 = send(cols(own, p ^ 3), xor_perm(nblk, 3))
    rest = jnp.concatenate([cols(own, p ^ 2 ^ m) for m in range(1, GROUP)], axis=2)
    rest, _, _ = lax.optimization_barrier((rest, c2, c3))
    rest = send(rest, xor_perm(nblk, 2))
    q2 = jnp.zeros_like(own)
    q2 = lax.dynamic_update_slice_in_dim(q2, c2, p * cw, axis=2)
    for m in range(1, GROUP):
        q2 = lax.dynamic_update_slice_in_dim(q2, rest[:, :, (m - 1) * cw:m * cw], (p ^ m) * cw, axis=2)
    q3 = send(q2, xor_perm(nblk, 1))

    def mm(lhs, rhs):
        return jnp.einsum(
            "aik,bkj->abij", lhs, rhs,
            precision=lax.Precision.HIGH, preferred_element_type=jnp.float32,
        )

    part_a = jnp.concatenate([cols(own, p), cols(q1, p)], axis=1)
    part_b = jnp.concatenate([c2, c3], axis=1)
    up = shift_perm(nblk, GROUP)
    dn = shift_perm(nblk, -GROUP)
    ua = send(part_a, up)
    da = send(part_a, dn)
    ub = send(part_b, up)
    db = send(part_b, dn)
    fa = send(ua, up)
    fb = send(db, dn)

    half = GROUP // 2
    pieces = [
        (y, 0, part_a), (y, 1, part_b),
        ((y - 1) % ny, 0, ua), ((y + 1) % ny, 0, da),
        ((y - 1) % ny, 1, ub), ((y + 1) % ny, 1, db),
        ((y + 2) % ny, 0, fa), ((y + 2) % ny, 1, fb),
    ]

    def kblk(g, m):
        return (GROUP * g + (p ^ m)) * rb

    early = jnp.concatenate([own, q1], axis=1)
    t_early = None
    for g, h, pc in pieces:
        lhs = jnp.concatenate(
            [lax.dynamic_slice_in_dim(early, kblk(g, half * h + i), rb, axis=2) for i in range(half)],
            axis=2,
        )
        term = mm(lhs, pc)
        t_early = term if t_early is None else t_early + term

    right = jnp.zeros((2, n, cw), jnp.float32)
    for g, h, pc in pieces:
        for i in range(half):
            right = lax.dynamic_update_slice_in_dim(
                right, pc[:, i * rb:(i + 1) * rb], kblk(g, half * h + i), axis=1
            )
    late = jnp.concatenate([q2, q3], axis=1)
    t_late = mm(late, right)
    t = jnp.concatenate([t_early, t_late], axis=2)

    prod_re = t[0, 0] - t[1, 1]
    prod_im = t[0, 1] + t[1, 0]
    scale = 1.0 / math.sqrt(n)
    w_re = signature[0, 0]
    w_im = signature[0, 1]
    out_re = -(w_re * prod_re - w_im * prod_im) * scale
    out_im = -(w_re * prod_im + w_im * prod_re) * scale
    blk_out = jnp.stack([out_re, out_im], axis=0)

    parts = [blk_out[:, :rb]]
    for m in range(1, GROUP):
        parts.append(send(blk_out[:, m * rb:(m + 1) * rb], xor_perm(nblk, m)))
    stacked = jnp.stack(parts, axis=0)
    ordered = [lax.dynamic_index_in_dim(stacked, p ^ i, 0, keepdims=False) for i in range(GROUP)]
    out = jnp.concatenate(ordered, axis=2)
    return out[None]


def solution(mesh):
    return jax.shard_map(
        on_device,
        mesh=mesh,
        in_specs=(P("blk", "freq", None), P("freq", None)),
        out_specs=P("freq", None, "blk", None),
        check_vma=False,
    )
```

```python
import math

import jax
import jax.numpy as jnp
from jax import lax
from jax.sharding import PartitionSpec as P


BIN0 = 4
BINSTEP = 3
GROUP = 4


def make_table(freqs, samples, first=0):
    bins = BIN0 + BINSTEP * ((first + jnp.arange(freqs, dtype=jnp.int32)) % freqs)
    steps = jnp.arange(samples, dtype=jnp.int32)
    phase = steps[:, None] * bins[None, :] % samples
    angle = phase.astype(jnp.float32) * (2.0 * math.pi / samples)
    scale = 1.0 / math.sqrt(samples)
    table = jnp.concatenate([jnp.cos(angle) * scale, -jnp.sin(angle) * scale], axis=1)
    return table.astype(jnp.bfloat16)


def xor_perm(n, m):
    return [(i, i ^ m) for i in range(n)]


def shift_perm(n, s):
    return [(i, (i + s) % n) for i in range(n)]


def send(x, perm):
    return lax.ppermute(x, "blk", perm)


def on_device(traces, signature):
    src_rows, rec_cols, samples = traces.shape
    freqs = lax.axis_size("freq")
    nblk = lax.axis_size("blk")
    ny = nblk // GROUP
    assert ny == 4 and nblk % GROUP == 0
    f = lax.axis_index("freq")
    table = make_table(freqs, samples, f)
    table = table.reshape(samples, 2, freqs).transpose(0, 2, 1).reshape(samples, 2 * freqs)
    projected = jnp.einsum("srt,tc->csr", traces, table, preferred_element_type=jnp.float32)
    projected = projected.reshape(freqs, 2, src_rows, rec_cols)
    own = jnp.zeros((2, src_rows, freqs * rec_cols), jnp.float32)
    own = lax.dynamic_update_slice_in_dim(own, projected[0], f * rec_cols, axis=2)
    for k in range(1, freqs):
        chunk = projected[k]
        got = lax.ppermute(chunk, "freq", shift_perm(freqs, k))
        own = lax.dynamic_update_slice_in_dim(own, got, ((f - k) % freqs) * rec_cols, axis=2)
    n = own.shape[2]
    rb = src_rows
    cw = n // GROUP

    b = lax.axis_index("blk")
    p = b % GROUP
    y = b // GROUP

    def cols(x, i):
        return lax.dynamic_slice_in_dim(x, i * cw, cw, axis=2)

    q1c = send(cols(own, p ^ 1), xor_perm(nblk, 1))
    q1 = send(own, xor_perm(nblk, 1))
    c2 = send(cols(own, p ^ 2), xor_perm(nblk, 2))
    c3 = send(cols(own, p ^ 3), xor_perm(nblk, 3))
    rest = jnp.concatenate([cols(own, p ^ 2 ^ m) for m in range(1, GROUP)], axis=2)
    rest, _, _ = lax.optimization_barrier((rest, c2, c3))
    rest = send(rest, xor_perm(nblk, 2))
    q2 = jnp.zeros_like(own)
    q2 = lax.dynamic_update_slice_in_dim(q2, c2, p * cw, axis=2)
    for m in range(1, GROUP):
        q2 = lax.dynamic_update_slice_in_dim(q2, rest[:, :, (m - 1) * cw:m * cw], (p ^ m) * cw, axis=2)
    q3 = send(q2, xor_perm(nblk, 1))

    def mm(lhs, rhs):
        return jnp.einsum(
            "aik,bkj->abij", lhs, rhs,
            precision=lax.Precision.HIGH, preferred_element_type=jnp.float32,
        )

    part_a = jnp.concatenate([cols(own, p), q1c], axis=1)
    part_b = jnp.concatenate([c2, c3], axis=1)
    up = shift_perm(nblk, GROUP)
    dn = shift_perm(nblk, -GROUP)
    ua = send(part_a, up)
    da = send(part_a, dn)
    ub = send(part_b, up)
    db = send(part_b, dn)
    fa = send(ua, up)
    fb = send(db, dn)

    half = GROUP // 2
    pieces = [
        (y, 0, part_a), (y, 1, part_b),
        ((y - 1) % ny, 0, ua), ((y + 1) % ny, 0, da),
        ((y - 1) % ny, 1, ub), ((y + 1) % ny, 1, db),
        ((y + 2) % ny, 0, fa), ((y + 2) % ny, 1, fb),
    ]

    def kblk(g, m):
        return (GROUP * g + (p ^ m)) * rb

    early = jnp.concatenate([own, q1], axis=1)
    t_early = None
    for g, h, pc in pieces:
        lhs = jnp.concatenate(
            [lax.dynamic_slice_in_dim(early, kblk(g, half * h + i), rb, axis=2) for i in range(half)],
            axis=2,
        )
        term = mm(lhs, pc)
        t_early = term if t_early is None else t_early + term

    right = jnp.zeros((2, n, cw), jnp.float32)
    for g, h, pc in pieces:
        for i in range(half):
            right = lax.dynamic_update_slice_in_dim(
                right, pc[:, i * rb:(i + 1) * rb], kblk(g, half * h + i), axis=1
            )
    late = jnp.concatenate([q2, q3], axis=1)
    t_late = mm(late, right)
    t = jnp.concatenate([t_early, t_late], axis=2)

    prod_re = t[0, 0] - t[1, 1]
    prod_im = t[0, 1] + t[1, 0]
    scale = 1.0 / math.sqrt(n)
    w_re = signature[0, 0]
    w_im = signature[0, 1]
    out_re = -(w_re * prod_re - w_im * prod_im) * scale
    out_im = -(w_re * prod_im + w_im * prod_re) * scale
    blk_out = jnp.stack([out_re, out_im], axis=0)

    out = lax.dynamic_update_slice_in_dim(jnp.zeros_like(own), blk_out[:, :rb], p * cw, axis=2)
    for m in range(1, GROUP):
        got = send(blk_out[:, m * rb:(m + 1) * rb], xor_perm(nblk, m))
        out = lax.dynamic_update_slice_in_dim(out, got, (p ^ m) * cw, axis=2)
    return out[None]


def solution(mesh):
    return jax.shard_map(
        on_device,
        mesh=mesh,
        in_specs=(P("blk", "freq", None), P("freq", None)),
        out_specs=P("freq", None, "blk", None),
        check_vma=False,
    )
```
